512 devices in a mesh: dom: 512 (over x, y, z, core).
Axes of the slice: x: 4, y: 8, z: 8, core: 2. Of those that a mesh axis runs over, the one named last changes fastest.
Arguments:
- q_state: float32 [9, 56, 65536], P(None, None, 'dom'), may hold values from -6 to 6
- star_mats: float32 [3, 9, 9, 65536], P(None, None, None, 'dom'), may hold values from -3 to 3
- flux_minus: float32 [4, 9, 9, 65536], P(None, None, None, 'dom'), may hold values from -2 to 2
- flux_plus: float32 [4, 9, 9, 65536], P(None, None, None, 'dom'), may hold values from -2 to 2
- time_limit: float32 [65536], P('dom'), may hold values from 0.25 to 3.6
- deriv_mats: float32 [3, 56, 56], replicated, may hold values from -0.75 to 0.75
- volume_mats: float32 [3, 56, 56], replicated, may hold values from -0.75 to 0.75
- face_proj: float32 [4, 21, 56], replicated, may hold values from -0.75 to 0.75
- face_lift: float32 [4, 56, 21], replicated, may hold values from -1.25 to 1.25
- face_link: int32 [4, 65536], P(None, 'dom'), may hold values from -1 to 895, as said below
- face_orient: int32 [4, 65536], P(None, 'dom'), may hold values from 0 to 2
- send_face: int32 [6, 32768], P(None, 'dom'), may hold values from -1 to 511, as said below
Outputs:
- q_new: float32 [9, 56, 65536], P(None, None, 'dom')
The draws below stay inside these ranges and needn't reach their ends.
Inputs may be any that keep to these rules, and one draw needn't show every extreme that they name: For face f of element e of a partition, v = face_link[f, d * 128 + e]: -1 is an absorbing boundary; v < 512 names face v // 128 of element v % 128 of the same partition; otherwise v = 512 + k * 64 + s names slot s of received block k, and s is below the number of faces that the partition at offset o_k sends it. No block holds more than 64 faces, and some blocks are full. `send_face`: row k of a partition's 64 columns lists the faces f * 128 + e that it sends to the partition at offset - o_k, then -1 in the unused slots; their number equals what that partition reads from the block; no face stands twice on a partition.
All inputs are finite; a program needn't handle non-finite values.
Results may differ from the reference program's by a relative error of at most 0.0003.
Values sent between devices are 32-bit elements; how exact they have to be, the bound alone decides.
No kernel may reach another device: no remote copies, remote signals or barrier semaphores. Data moves between devices by JAX's collectives and lax.ppermute only.
A program may use at most 128 MiB of HBM per device.

```python
import math
import jax
import jax.numpy as jnp
import numpy as np
from jax import lax

NQ = 9
NB = 56
NF = 21
ORDER = 6
REACH = 3
SCAP = 64
FINE_DEV = 64
NOFF = 6
E_DEV = 128
ELEMS = 65536
N_DOM = 512


def block_offsets():
    return jnp.array([position - REACH if position < REACH else position - REACH + 1 for position in range(NOFF)], dtype=jnp.int32)


def mesh_links(key):
    base_key = jax.random.fold_in(key, 7103)
    device_ids = jnp.arange(N_DOM, dtype=jnp.int32)
    offsets = block_offsets()
    source = device_ids[:, None] + offsets[None, :]
    present = (source >= 0) & (source < N_DOM)
    raw_counts = jax.random.randint(jax.random.fold_in(base_key, 1), (N_DOM, NOFF), SCAP // 4, SCAP + 1, dtype=jnp.int32)
    filled = (device_ids[:, None] + jnp.arange(NOFF, dtype=jnp.int32)[None, :]) % 3 == 0
    counts = jnp.where(present, jnp.where(filled, SCAP, raw_counts), 0).astype(jnp.int32)
    face_total = 4 * E_DEV
    positions = jnp.arange(face_total, dtype=jnp.int32)

    def receiver(device_key, row_counts):
        perm_key, local_key = jax.random.split(device_key)
        placing = jax.random.permutation(perm_key, face_total).astype(jnp.int32)
        block_ends = jnp.cumsum(row_counts).astype(jnp.int32)
        block_starts = block_ends - row_counts
        block_index = jnp.minimum(jnp.sum((positions[:, None] >= block_ends[None, :]).astype(jnp.int32), axis=1), NOFF - 1)
        remote = face_total + block_index * SCAP + positions - block_starts[block_index]
        local_link = jax.random.randint(local_key, (face_total,), 0, face_total, dtype=jnp.int32)
        remote_total = block_ends[NOFF - 1]
        link_value = jnp.where(positions < remote_total, remote, jnp.where(positions < remote_total + E_DEV // 4, -1, local_link))
        inverse = jnp.argsort(placing)
        return link_value[inverse].reshape(4, E_DEV).astype(jnp.int32)
    receive_keys = jax.vmap(lambda number: jax.random.fold_in(jax.random.fold_in(base_key, 2), number))(device_ids)
    link_table = jax.vmap(receiver)(receive_keys, counts)
    target = device_ids[:, None] - offsets[None, :]
    target_valid = (target >= 0) & (target < N_DOM)
    send_counts = jnp.where(target_valid, counts[jnp.clip(target, 0, N_DOM - 1), jnp.arange(NOFF, dtype=jnp.int32)[None, :]], 0)

    def sender(device_key, row_counts):
        chosen = jax.random.permutation(device_key, face_total).astype(jnp.int32)[:NOFF * SCAP].reshape(NOFF, SCAP)
        slot_index = jnp.arange(SCAP, dtype=jnp.int32)[None, :]
        return jnp.where(slot_index < row_counts[:, None], chosen, -1).astype(jnp.int32)
    send_keys = jax.vmap(lambda number: jax.random.fold_in(jax.random.fold_in(base_key, 3), number))(device_ids)
    send_table = jax.vmap(sender)(send_keys, send_counts)
    links_out = jnp.transpose(link_table, (1, 0, 2)).reshape(4, N_DOM * E_DEV)
    sends_out = jnp.transpose(send_table, (1, 0, 2)).reshape(NOFF, N_DOM * SCAP)
    return (links_out, sends_out)


def draw_face_link(key, part):
    return mesh_links(key)[0]


def draw_send_face(key, part):
    return mesh_links(key)[1]


def draw_time_limit(key, part):
    device_key, element_key = jax.random.split(key)
    device_pos = jnp.arange(N_DOM, dtype=jnp.float32)[:, None] / max(N_DOM - 1, 1)
    cluster = jnp.where(jnp.arange(E_DEV)[None, :] < FINE_DEV, 1.0, 2.0)
    device_factor = jnp.exp(math.log(2.0) * jax.random.uniform(device_key, (N_DOM, 1), jnp.float32))
    element_factor = 1.0 + 0.2 * jax.random.uniform(element_key, (N_DOM, E_DEV), jnp.float32)
    limits = 0.25 * cluster * (1.0 + 2.0 * device_pos) * device_factor * element_factor
    return limits.reshape(N_DOM * E_DEV).astype(jnp.float32)


def set_ends(entries, own_key, least, largest):
    spot = [jax.random.randint(jax.random.fold_in(own_key, axis), (), 0, length) for axis, length in enumerate(entries.shape)]
    longest = entries.shape.index(max(entries.shape))
    beside = spot[:longest] + [(spot[longest] + 1) % entries.shape[longest]] + spot[longest + 1:]
    return entries.at[tuple(spot)].set(least).at[tuple(beside)].set(largest)


def shard_levels(own_key, shape, cuts, low, largest):
    factor_of, own = 1.0, jax.random.fold_in(own_key, 6)
    for dim, shards_of in cuts:
        draws = jnp.exp(jax.random.uniform(jax.random.fold_in(own, dim), (shards_of,), jnp.float32, low / len(cuts), largest / len(cuts)))
        factor_of = factor_of * jnp.repeat(draws, shape[dim] // shards_of).reshape([-1 if axis == dim else 1 for axis in range(len(shape))])
    return factor_of


def normal_values(key, extent, width, reach, shards=(), kind=jnp.bfloat16):
    drawn = width * jax.random.normal(key, extent, jnp.float32)
    if shards:
        drawn = drawn * shard_levels(key, extent, shards, -0.22, 0.18)
    return jnp.clip(drawn, -reach, reach).astype(kind)


def setup_inputs(seed: int = 0) -> dict:
    arg_keys = jax.random.split(jax.random.key(seed), 13)
    q_state = normal_values(arg_keys[0], (NQ, NB, ELEMS), 1.0, 6.0, ((2, 512),), jnp.float32)
    star_mats = normal_values(arg_keys[1], (3, NQ, NQ, ELEMS), 0.6, 3.0, ((3, 512),), jnp.float32)
    flux_minus = normal_values(arg_keys[2], (4, NQ, NQ, ELEMS), NQ ** -0.5, 2.0, ((3, 512),), jnp.float32)
    flux_plus = normal_values(arg_keys[3], (4, NQ, NQ, ELEMS), NQ ** -0.5, 2.0, ((3, 512),), jnp.float32)
    time_limit = draw_time_limit(jax.random.fold_in(arg_keys[12], 71), 0)
    deriv_mats = normal_values(arg_keys[5], (3, NB, NB), NB ** -0.5, 0.75, (), jnp.float32)
    volume_mats = normal_values(arg_keys[6], (3, NB, NB), NB ** -0.5, 0.75, (), jnp.float32)
    face_proj = normal_values(arg_keys[7], (4, NF, NB), NB ** -0.5, 0.75, (), jnp.float32)
    face_lift = normal_values(arg_keys[8], (4, NB, NF), NF ** -0.5, 1.25, (), jnp.float32)
    face_link = draw_face_link(jax.random.fold_in(arg_keys[12], 71), 0)
    face_orient = set_ends(jax.random.randint(arg_keys[10], (4, ELEMS), 0, 3), jax.random.fold_in(arg_keys[10], 1), 0, 2).astype(jnp.int32)
    send_face = draw_send_face(jax.random.fold_in(arg_keys[12], 71), 0)
    return {"q_state": q_state, "star_mats": star_mats, "flux_minus": flux_minus, "flux_plus": flux_plus, "time_limit": time_limit, "deriv_mats": deriv_mats, "volume_mats": volume_mats, "face_proj": face_proj, "face_lift": face_lift, "face_link": face_link, "face_orient": face_orient, "send_face": send_face}


HIGH = lax.Precision.HIGHEST
STEP_RATIO = 2.0


def rotation_table(node_count):
    degree = 0
    while (degree + 1) * (degree + 2) // 2 < node_count:
        degree += 1
    node_pairs = [(across, upward) for across in range(degree + 1) for upward in range(degree + 1 - across)]
    lookup = {}
    for number, node_pair in enumerate(node_pairs):
        lookup[node_pair] = number
    tables = []
    for rotations in range(3):
        new_order = []
        for node_pair in node_pairs:
            moved_pair = (node_pair[1], node_pair[0])
            for repeat in range(rotations):
                moved_pair = (moved_pair[1], degree - moved_pair[0] - moved_pair[1])
            new_order.append(lookup[moved_pair])
        tables.append(new_order)
    return np.array(tables, dtype=np.int32)


def taylor_series(coeffs, star_part, deriv_mats):
    series = [coeffs]
    current = coeffs
    for term_index in range(ORDER - 1):
        derived = jnp.einsum('dbc,qce->dbqe', deriv_mats, current, precision=HIGH)
        current = -jnp.sum(star_part[:, :, :, None, :] * jnp.swapaxes(derived, 1, 2)[:, None, :, :, :], axis=(0, 2))
        series.append(current)
    return series


def integrate(series, start_time, end_time):
    summed = (end_time - start_time) * series[0]
    for term_index in range(1, len(series)):
        weight = (end_time ** (term_index + 1) - start_time ** (term_index + 1)) / math.factorial(term_index + 1)
        summed = summed + weight * series[term_index]
    return summed


def face_values(integral, face_proj):
    projected = jnp.einsum('fnb,qbe->qnfe', face_proj, integral, precision=HIGH)
    return projected.reshape(projected.shape[0], projected.shape[1], -1)


def neighbour_faces(face_pool, face_links, orients, rotation):
    face_count = face_links.shape[0] * face_links.shape[1]
    padded = jnp.concatenate([face_pool, jnp.zeros((face_pool.shape[0], face_pool.shape[1], 1), face_pool.dtype)], axis=2)
    indices = jnp.where(face_links < 0, face_pool.shape[2], face_links).reshape(face_count)
    picked = jnp.take(padded, indices, axis=2)
    orient_codes = orients.reshape(face_count)
    turned = jnp.where(orient_codes == 0, picked[:, rotation[0], :],
                       jnp.where(orient_codes == 1, picked[:, rotation[1], :], picked[:, rotation[2], :]))
    return turned.reshape(face_pool.shape[0], face_pool.shape[1], face_links.shape[0], face_links.shape[1])


def face_flux(solver_part, face_data):
    moved = jnp.transpose(face_data, (2, 0, 1, 3))
    return jnp.sum(solver_part[:, :, :, None, :] * moved[:, None, :, :, :], axis=2)


def advance(coeffs, integral, own_faces, neighbour, star_part, volume_mats, face_lift, minus_part, plus_part):
    starred = jnp.sum(star_part[:, :, :, None, :] * integral[None, None, :, :, :], axis=2)
    gained = jnp.einsum('dbc,dpce->pbe', volume_mats, starred, precision=HIGH)
    across = face_flux(minus_part, own_faces) + face_flux(plus_part, neighbour)
    lifted = jnp.einsum('fbn,fpne->pbe', face_lift, across, precision=HIGH)
    return coeffs + gained - lifted


def pack_blocks(faces_flat, sends):
    padded = jnp.concatenate([faces_flat, jnp.zeros((faces_flat.shape[0], faces_flat.shape[1], 1), faces_flat.dtype)], axis=2)
    indices = jnp.where(sends < 0, faces_flat.shape[2], sends).reshape(sends.shape[0] * sends.shape[1])
    picked = jnp.take(padded, indices, axis=2)
    return picked.reshape(faces_flat.shape[0], faces_flat.shape[1], sends.shape[0], sends.shape[1])


def route(send_blocks):
    device_ids = jnp.arange(N_DOM)
    gathered = []
    for position in range(NOFF):
        offset = position - REACH if position < REACH else position - REACH + 1
        rolled = jnp.roll(send_blocks[:, :, :, position, :], -offset, axis=0)
        present = (device_ids + offset >= 0) & (device_ids + offset < N_DOM)
        gathered.append(jnp.where(present[:, None, None, None], rolled, 0.0))
    stacked = jnp.stack(gathered, axis=3)
    return stacked.reshape(N_DOM, NQ, NF, NOFF * SCAP)


def reference(q_state, star_mats, flux_minus, flux_plus, time_limit, deriv_mats, volume_mats, face_proj, face_lift, face_link, face_orient, send_face):
    rotation = rotation_table(NF)

    def by_device(array):
        shaped = array.reshape(array.shape[:-1] + (N_DOM, E_DEV))
        return jnp.moveaxis(shaped, -2, 0)

    coeff_all = by_device(q_state)
    star_all = by_device(star_mats)
    minus_all = by_device(flux_minus)
    plus_all = by_device(flux_plus)
    link_all = by_device(face_link)
    orient_all = by_device(face_orient)
    send_all = jnp.moveaxis(send_face.reshape(NOFF, N_DOM, SCAP), 1, 0)
    local_index = jnp.arange(ELEMS) % E_DEV
    allowed = jnp.where(local_index < FINE_DEV, time_limit, time_limit / STEP_RATIO)
    step_fine = jnp.min(allowed)
    step_coarse = STEP_RATIO * step_fine

    def device_work(device_item, depth):
        coeffs, star_dev, minus_dev, plus_dev, links, orients, sends, received_one, received_two = device_item
        fine_star = star_dev[..., :FINE_DEV]
        coarse_star = star_dev[..., FINE_DEV:]
        fine_series = taylor_series(coeffs[:, :, :FINE_DEV], fine_star, deriv_mats)
        coarse_series = taylor_series(coeffs[:, :, FINE_DEV:], coarse_star, deriv_mats)
        fine_one = integrate(fine_series, 0.0, step_fine)
        coarse_one = integrate(coarse_series, 0.0, step_fine)
        coarse_two = integrate(coarse_series, step_fine, step_coarse)
        faces_one = face_values(jnp.concatenate([fine_one, coarse_one], axis=2), face_proj)
        if depth == 1:
            return pack_blocks(faces_one, sends)
        fine_links = links[:, :FINE_DEV]
        fine_orients = orients[:, :FINE_DEV]
        fine_minus = minus_dev[..., :FINE_DEV]
        fine_plus = plus_dev[..., :FINE_DEV]
        shaped_one = faces_one.reshape(NQ, NF, 4, E_DEV)
        pool_one = jnp.concatenate([faces_one, received_one], axis=2)
        fine_mid = advance(coeffs[:, :, :FINE_DEV], fine_one, shaped_one[..., :FINE_DEV],
                           neighbour_faces(pool_one, fine_links, fine_orients, rotation),
                           fine_star, volume_mats, face_lift, fine_minus, fine_plus)
        fine_two = integrate(taylor_series(fine_mid, fine_star, deriv_mats), 0.0, step_fine)
        faces_two = face_values(jnp.concatenate([fine_two, coarse_two], axis=2), face_proj)
        if depth == 2:
            return pack_blocks(faces_two, sends)
        shaped_two = faces_two.reshape(NQ, NF, 4, E_DEV)
        pool_two = jnp.concatenate([faces_two, received_two], axis=2)
        fine_end = advance(fine_mid, fine_two, shaped_two[..., :FINE_DEV],
                           neighbour_faces(pool_two, fine_links, fine_orients, rotation),
                           fine_star, volume_mats, face_lift, fine_minus, fine_plus)
        pool_both = jnp.concatenate([faces_one + faces_two, received_one + received_two], axis=2)
        coarse_end = advance(coeffs[:, :, FINE_DEV:], coarse_one + coarse_two, (shaped_one + shaped_two)[..., FINE_DEV:],
                             neighbour_faces(pool_both, links[:, FINE_DEV:], orients[:, FINE_DEV:], rotation),
                             coarse_star, volume_mats, face_lift, minus_dev[..., FINE_DEV:], plus_dev[..., FINE_DEV:])
        return jnp.concatenate([fine_end, coarse_end], axis=2)

    blank = jnp.zeros((N_DOM, NQ, NF, NOFF * SCAP), jnp.float32)
    common = (coeff_all, star_all, minus_all, plus_all, link_all, orient_all, send_all)
    sends_one = lax.map(lambda device_item: device_work(device_item, 1), common + (blank, blank))
    received_one = route(sends_one)
    sends_two = lax.map(lambda device_item: device_work(device_item, 2), common + (received_one, blank))
    received_two = route(sends_two)
    updated = lax.map(lambda device_item: device_work(device_item, 3), common + (received_one, received_two))
    return jnp.moveaxis(updated, 0, -2).reshape(NQ, NB, ELEMS)
```

```python
import math

import jax
import jax.numpy as jnp
import numpy as np
from jax import lax
from jax.sharding import PartitionSpec as P

ORDER = 6
REACH = 3
FINE_DEV = 64


HIGH = lax.Precision.HIGHEST
STEP_RATIO = 2.0


def passed_along(value, axis, steps):
    count = lax.axis_size(axis)
    leading, last = (max(0, -steps), min(count, count - steps))
    return lax.ppermute(value, axis, [(source, source + steps) for source in range(leading, last)])


def global_min(value, axis):
    count = lax.axis_size(axis)
    if count & (count - 1):
        return lax.pmin(value, axis)
    stride = 1
    while stride < count:
        partner = lax.ppermute(value, axis, [(source, source ^ stride) for source in range(count)])
        value = jnp.minimum(value, partner)
        stride *= 2
    return value


def rotation_table(node_count):
    degree = 0
    while (degree + 1) * (degree + 2) // 2 < node_count:
        degree += 1
    node_pairs = [
        (across, upward) for across in range(degree + 1) for upward in range(degree + 1 - across)
    ]
    lookup = {}
    for number, node_pair in enumerate(node_pairs):
        lookup[node_pair] = number
    tables = []
    for rotations in range(3):
        new_order = []
        for node_pair in node_pairs:
            moved_pair = (node_pair[1], node_pair[0])
            for repeat in range(rotations):
                moved_pair = (moved_pair[1], degree - moved_pair[0] - moved_pair[1])
            new_order.append(lookup[moved_pair])
        tables.append(new_order)
    return np.array(tables, dtype=np.int32)


def taylor_series(coeffs, star_part, deriv_mats):
    series = [coeffs]
    current = coeffs
    for term_index in range(ORDER - 1):
        derived = jnp.einsum("dbc,qce->dbqe", deriv_mats, current, precision=HIGH)
        current = -jnp.sum(
            star_part[:, :, :, None, :] * jnp.swapaxes(derived, 1, 2)[:, None, :, :, :], axis=(0, 2)
        )
        series.append(current)
    return series


def integrate(series, start_time, end_time):
    summed = (end_time - start_time) * series[0]
    for term_index in range(1, len(series)):
        weight = (end_time ** (term_index + 1) - start_time ** (term_index + 1)) / math.factorial(
            term_index + 1
        )
        summed = summed + weight * series[term_index]
    return summed


def face_values(integral, face_proj):
    return jnp.einsum("fnb,qbe->qnfe", face_proj, integral, precision=HIGH)


def one_hot(indices, count):
    flat = indices.reshape(-1)
    return (lax.broadcasted_iota(jnp.int32, (count, flat.shape[0]), 0) == flat[None, :]).astype(
        jnp.float32
    )


def pick_columns(values, selector):
    return jnp.einsum("qnc,cx->qnx", values, selector, precision=HIGH)


def rotate(picked, orients, rotation):
    codes = orients.reshape(-1)
    return jnp.where(
        codes == 0,
        picked[:, rotation[0], :],
        jnp.where(codes == 1, picked[:, rotation[1], :], picked[:, rotation[2], :]),
    )


def route(send_blocks, blocks):
    received = []
    for position in range(2 * REACH):
        offset = position - REACH if position < REACH else position - REACH + 1
        received.append(passed_along(send_blocks[:, :, position * blocks : (position + 1) * blocks], "dom", -offset))
    return jnp.concatenate(received, axis=2)


def face_flux(solver_part, face_data):
    moved = jnp.transpose(face_data, (2, 0, 1, 3))
    return jnp.sum(solver_part[:, :, :, None, :] * moved[:, None, :, :, :], axis=2)


def advance(
    coeffs, integral, own_faces, neighbour, star_part, volume_mats, face_lift, minus_part, plus_part
):
    starred = jnp.sum(star_part[:, :, :, None, :] * integral[None, None, :, :, :], axis=2)
    gained = jnp.einsum("dbc,dpce->pbe", volume_mats, starred, precision=HIGH)
    across = face_flux(minus_part, own_faces) + face_flux(plus_part, neighbour)
    lifted = jnp.einsum("fbn,fpne->pbe", face_lift, across, precision=HIGH)
    return coeffs + gained - lifted


def local(
    q_state,
    star_mats,
    flux_minus,
    flux_plus,
    time_limit,
    deriv_mats,
    volume_mats,
    face_proj,
    face_lift,
    face_link,
    face_orient,
    send_face,
):
    rotation = rotation_table(face_proj.shape[1])
    quantity = q_state.shape[0]
    face_nodes = face_proj.shape[1]
    elem_count = q_state.shape[2]
    face_count = face_link.shape[0]
    own_cols = face_count * elem_count
    blocks = send_face.shape[1]
    fine = FINE_DEV
    allowed = jnp.where(jnp.arange(elem_count) < fine, time_limit, time_limit / STEP_RATIO)
    step_fine = global_min(jnp.min(allowed), "dom")
    step_coarse = STEP_RATIO * step_fine

    series = taylor_series(q_state, star_mats, deriv_mats)
    first = integrate(series, 0.0, step_fine)
    coarse_two = integrate([term[:, :, fine:] for term in series], step_fine, step_coarse)

    faces_one = face_values(first, face_proj)
    flat_one = faces_one.reshape(quantity, face_nodes, own_cols)
    send_pick = one_hot(send_face, own_cols)
    received_one = route(pick_columns(flat_one, send_pick), blocks)

    fine_links = face_link[:, :fine]
    fine_orients = face_orient[:, :fine]
    fine_star = star_mats[..., :fine]
    fine_minus = flux_minus[..., :fine]
    fine_plus = flux_plus[..., :fine]
    pool_cols = own_cols + received_one.shape[2]
    fine_pick = one_hot(fine_links, pool_cols)
    picked_one = pick_columns(flat_one, fine_pick[:own_cols]) + pick_columns(
        received_one, fine_pick[own_cols:]
    )
    neighbour_one = rotate(picked_one, fine_orients, rotation).reshape(
        quantity, face_nodes, face_count, fine
    )
    fine_mid = advance(
        q_state[:, :, :fine],
        first[:, :, :fine],
        faces_one[..., :fine],
        neighbour_one,
        fine_star,
        volume_mats,
        face_lift,
        fine_minus,
        fine_plus,
    )
    fine_two = integrate(taylor_series(fine_mid, fine_star, deriv_mats), 0.0, step_fine)
    second = jnp.concatenate([fine_two, coarse_two], axis=2)
    faces_two = face_values(second, face_proj)
    flat_two = faces_two.reshape(quantity, face_nodes, own_cols)
    received_two = route(pick_columns(flat_two, send_pick), blocks)

    is_fine = jnp.arange(elem_count) < fine
    all_pick = one_hot(face_link, pool_cols)
    coarse_pick = all_pick * jnp.tile(jnp.logical_not(is_fine), face_count)[None, :].astype(jnp.float32)
    picked_end = (
        pick_columns(flat_two, all_pick[:own_cols])
        + pick_columns(received_two, all_pick[own_cols:])
        + pick_columns(flat_one, coarse_pick[:own_cols])
        + pick_columns(received_one, coarse_pick[own_cols:])
    )
    neighbour_end = rotate(picked_end, face_orient, rotation).reshape(
        quantity, face_nodes, face_count, elem_count
    )
    own_end = jnp.where(is_fine, faces_two, faces_one + faces_two)
    coeffs_end = jnp.concatenate([fine_mid, q_state[:, :, fine:]], axis=2)
    integral_end = jnp.concatenate([fine_two, first[:, :, fine:] + coarse_two], axis=2)
    return advance(
        coeffs_end,
        integral_end,
        own_end,
        neighbour_end,
        star_mats,
        volume_mats,
        face_lift,
        flux_minus,
        flux_plus,
    )


def solution(mesh):
    placed = (
        P(None, None, "dom"),
        P(None, None, None, "dom"),
        P(None, None, None, "dom"),
        P(None, None, None, "dom"),
        P("dom"),
        P(),
        P(),
        P(),
        P(),
        P(None, "dom"),
        P(None, "dom"),
        P(None, "dom"),
    )
    return jax.shard_map(
        local, mesh=mesh, in_specs=placed, out_specs=P(None, None, "dom"), check_vma=False
    )
```

```python
import math

import jax
import jax.numpy as jnp
import numpy as np
from jax import lax
from jax.sharding import PartitionSpec as P

ORDER = 6
REACH = 3
FINE_DEV = 64


HIGH = lax.Precision.HIGHEST
STEP_RATIO = 2.0


def passed_along(value, axis, steps):
    count = lax.axis_size(axis)
    leading, last = (max(0, -steps), min(count, count - steps))
    return lax.ppermute(value, axis, [(source, source + steps) for source in range(leading, last)])


def global_min(value, axis, state, steps):
    count = lax.axis_size(axis)
    taken = 0
    if count & (count - 1):
        value = lax.pmin(value, axis)
    stride = 1
    while stride < count and not count & (count - 1):
        partner = lax.ppermute(value, axis, [(source, source ^ stride) for source in range(count)])
        if taken < len(steps):
            state = steps[taken](state)
            partner, state = lax.optimization_barrier((partner, state))
            taken += 1
        value = jnp.minimum(value, partner)
        stride *= 2
    for step in steps[taken:]:
        state = step(state)
    return value, state


def rotation_table(node_count):
    degree = 0
    while (degree + 1) * (degree + 2) // 2 < node_count:
        degree += 1
    node_pairs = [
        (across, upward) for across in range(degree + 1) for upward in range(degree + 1 - across)
    ]
    lookup = {}
    for number, node_pair in enumerate(node_pairs):
        lookup[node_pair] = number
    tables = []
    for rotations in range(3):
        new_order = []
        for node_pair in node_pairs:
            moved_pair = (node_pair[1], node_pair[0])
            for repeat in range(rotations):
                moved_pair = (moved_pair[1], degree - moved_pair[0] - moved_pair[1])
            new_order.append(lookup[moved_pair])
        tables.append(new_order)
    return np.array(tables, dtype=np.int32)


def taylor_series(coeffs, star_part, deriv_mats):
    series = [coeffs]
    current = coeffs
    for term_index in range(ORDER - 1):
        derived = jnp.einsum("dbc,qce->dbqe", deriv_mats, current, precision=HIGH)
        current = -jnp.sum(
            star_part[:, :, :, None, :] * jnp.swapaxes(derived, 1, 2)[:, None, :, :, :], axis=(0, 2)
        )
        series.append(current)
    return series


def integrate(series, start_time, end_time):
    summed = (end_time - start_time) * series[0]
    for term_index in range(1, len(series)):
        weight = (end_time ** (term_index + 1) - start_time ** (term_index + 1)) / math.factorial(
            term_index + 1
        )
        summed = summed + weight * series[term_index]
    return summed


def series_step(star_part, deriv_mats):
    def step(state):
        current = state[-1]
        derived = jnp.einsum("dbc,qce->dbqe", deriv_mats, current, precision=HIGH)
        following = -jnp.sum(
            star_part[:, :, :, None, :] * jnp.swapaxes(derived, 1, 2)[:, None, :, :, :], axis=(0, 2)
        )
        return state + (following,)

    return step


def weights(start_time, end_time):
    out = [end_time - start_time]
    for term_index in range(1, ORDER):
        out.append(
            (end_time ** (term_index + 1) - start_time ** (term_index + 1))
            / math.factorial(term_index + 1)
        )
    return out


def combine(terms, factors):
    summed = factors[0] * terms[0]
    for term_index in range(1, len(factors)):
        summed = summed + factors[term_index] * terms[term_index]
    return summed


def face_values(integral, face_proj):
    return jnp.einsum("fnb,qbe->qnfe", face_proj, integral, precision=HIGH)


def one_hot(indices, count):
    flat = indices.reshape(-1)
    return (lax.broadcasted_iota(jnp.int32, (count, flat.shape[0]), 0) == flat[None, :]).astype(
        jnp.float32
    )


def pick_columns(values, selector):
    return jnp.einsum("qnc,cx->qnx", values, selector, precision=HIGH)


def route(send_blocks, blocks):
    received = []
    for position in range(2 * REACH):
        offset = position - REACH if position < REACH else position - REACH + 1
        part = send_blocks[:, :, position * blocks : (position + 1) * blocks]
        received.append(passed_along(part, "dom", -offset))
    return jnp.concatenate(received, axis=2)


def face_flux(solver_part, face_data):
    moved = jnp.transpose(face_data, (2, 0, 1, 3))
    return jnp.sum(solver_part[:, :, :, None, :] * moved[:, None, :, :, :], axis=2)


def advance(
    coeffs, integral, own_faces, picked, masks, star_part, volume_mats, face_lift, turned_lift,
    minus_part, plus_part,
):
    starred = jnp.sum(star_part[:, :, :, None, :] * integral[None, None, :, :, :], axis=2)
    gained = jnp.einsum("dbc,dpce->pbe", volume_mats, starred, precision=HIGH)
    own_flux = face_flux(minus_part, own_faces)
    far_flux = face_flux(plus_part, picked)
    masked = masks[:, :, None, None, :] * far_flux[None]
    lifted = jnp.einsum("fbn,fpne->pbe", face_lift, own_flux, precision=HIGH) + jnp.einsum(
        "hfbm,hfpme->pbe", turned_lift, masked, precision=HIGH
    )
    return coeffs + gained - lifted


def local(
    q_state,
    star_mats,
    flux_minus,
    flux_plus,
    time_limit,
    deriv_mats,
    volume_mats,
    face_proj,
    face_lift,
    face_link,
    face_orient,
    send_face,
):
    rotation = rotation_table(face_proj.shape[1])
    inverse = np.argsort(rotation, axis=1)
    turned_lift = jnp.stack([face_lift[:, :, inverse[turn]] for turn in range(3)])
    quantity = q_state.shape[0]
    face_nodes = face_proj.shape[1]
    elem_count = q_state.shape[2]
    face_count = face_link.shape[0]
    own_cols = face_count * elem_count
    blocks = send_face.shape[1]
    fine = FINE_DEV
    send_pick = one_hot(send_face, own_cols)
    send_rows = send_pick.reshape(face_count, elem_count, send_pick.shape[1])

    def project_terms(state):
        stacked = jnp.stack(state)
        faces = jnp.einsum("fnb,kqbe->kqnfe", face_proj, stacked, precision=HIGH)
        return state + (faces,)

    def pack_terms(state):
        faces = state[-1]
        sends = jnp.einsum(
            "kqnc,cs->kqns", faces.reshape(faces.shape[:3] + (own_cols,)), send_pick, precision=HIGH
        )
        coarse_sends = jnp.einsum(
            "kqnfe,fes->kqns", faces[..., fine:], send_rows[:, fine:], precision=HIGH
        )
        return state + (sends, coarse_sends)

    allowed = jnp.where(jnp.arange(elem_count) < fine, time_limit, time_limit / STEP_RATIO)
    steps = [series_step(star_mats, deriv_mats)] * (ORDER - 1) + [project_terms, pack_terms]
    step_fine, state = global_min(jnp.min(allowed), "dom", (q_state,), steps)
    series = state[:ORDER]
    face_terms, send_terms, coarse_send_terms = state[ORDER:]
    step_coarse = STEP_RATIO * step_fine
    first_weights = weights(0.0, step_fine)
    second_weights = weights(step_fine, step_coarse)

    received_one = route(combine(send_terms, first_weights), blocks)
    first = combine(series, first_weights)
    coarse_two = combine([term[:, :, fine:] for term in series], second_weights)
    faces_one = combine(face_terms, first_weights)
    flat_one = faces_one.reshape(quantity, face_nodes, own_cols)

    fine_star = star_mats[..., :fine]
    fine_minus = flux_minus[..., :fine]
    fine_plus = flux_plus[..., :fine]
    pool_cols = own_cols + received_one.shape[2]
    masks = jnp.stack([(face_orient == turn).astype(jnp.float32) for turn in range(3)])
    fine_pick = one_hot(face_link[:, :fine], pool_cols)
    picked_one = pick_columns(flat_one, fine_pick[:own_cols]) + pick_columns(
        received_one, fine_pick[own_cols:]
    )
    fine_mid = advance(
        q_state[:, :, :fine],
        first[:, :, :fine],
        faces_one[..., :fine],
        picked_one.reshape(quantity, face_nodes, face_count, fine),
        masks[..., :fine],
        fine_star,
        volume_mats,
        face_lift,
        turned_lift,
        fine_minus,
        fine_plus,
    )
    fine_state = (fine_mid,)
    for term_index in range(ORDER - 1):
        fine_state = series_step(fine_star, deriv_mats)(fine_state)
    fine_two = combine(fine_state, first_weights)
    fine_faces_two = face_values(fine_two, face_proj)
    sends_two = jnp.einsum(
        "qnfe,fes->qns", fine_faces_two, send_rows[:, :fine], precision=HIGH
    ) + combine(coarse_send_terms, second_weights)
    received_two = route(sends_two, blocks)
    coarse_faces_two = combine([faces[..., fine:] for faces in face_terms], second_weights)
    faces_two = jnp.concatenate([fine_faces_two, coarse_faces_two], axis=3)
    flat_two = faces_two.reshape(quantity, face_nodes, own_cols)

    is_fine = jnp.arange(elem_count) < fine
    all_pick = one_hot(face_link, pool_cols)
    coarse_pick = all_pick * jnp.tile(jnp.logical_not(is_fine), face_count)[None, :].astype(
        jnp.float32
    )
    picked_end = (
        pick_columns(flat_two, all_pick[:own_cols])
        + pick_columns(received_two, all_pick[own_cols:])
        + pick_columns(flat_one, coarse_pick[:own_cols])
        + pick_columns(received_one, coarse_pick[own_cols:])
    )
    own_end = jnp.where(is_fine, faces_two, faces_one + faces_two)
    coeffs_end = jnp.concatenate([fine_mid, q_state[:, :, fine:]], axis=2)
    integral_end = jnp.concatenate([fine_two, first[:, :, fine:] + coarse_two], axis=2)
    return advance(
        coeffs_end,
        integral_end,
        own_end,
        picked_end.reshape(quantity, face_nodes, face_count, elem_count),
        masks,
        star_mats,
        volume_mats,
        face_lift,
        turned_lift,
        flux_minus,
        flux_plus,
    )


def solution(mesh):
    placed = (
        P(None, None, "dom"),
        P(None, None, None, "dom"),
        P(None, None, None, "dom"),
        P(None, None, None, "dom"),
        P("dom"),
        P(),
        P(),
        P(),
        P(),
        P(None, "dom"),
        P(None, "dom"),
        P(None, "dom"),
    )
    return jax.shard_map(
        local, mesh=mesh, in_specs=placed, out_specs=P(None, None, "dom"), check_vma=False
    )
```

```python
import math

import jax
import jax.numpy as jnp
import numpy as np
from jax import lax
from jax.sharding import PartitionSpec as P

ORDER = 6
REACH = 3
FINE_DEV = 64


HIGH = lax.Precision.HIGHEST
STEP_RATIO = 2.0


def passed_along(value, axis, steps):
    count = lax.axis_size(axis)
    leading, last = (max(0, -steps), min(count, count - steps))
    return lax.ppermute(value, axis, [(source, source + steps) for source in range(leading, last)])


def global_min(value, axis):
    count = lax.axis_size(axis)
    if count & (count - 1):
        return lax.pmin(value, axis)
    stride = 1
    while stride < count:
        partner = lax.ppermute(value, axis, [(source, source ^ stride) for source in range(count)])
        value = jnp.minimum(value, partner)
        stride *= 2
    return value


def rotation_table(node_count):
    degree = 0
    while (degree + 1) * (degree + 2) // 2 < node_count:
        degree += 1
    node_pairs = [
        (across, upward) for across in range(degree + 1) for upward in range(degree + 1 - across)
    ]
    lookup = {}
    for number, node_pair in enumerate(node_pairs):
        lookup[node_pair] = number
    tables = []
    for rotations in range(3):
        new_order = []
        for node_pair in node_pairs:
            moved_pair = (node_pair[1], node_pair[0])
            for repeat in range(rotations):
                moved_pair = (moved_pair[1], degree - moved_pair[0] - moved_pair[1])
            new_order.append(lookup[moved_pair])
        tables.append(new_order)
    return np.array(tables, dtype=np.int32)


def taylor_series(coeffs, star_part, deriv_mats):
    series = [coeffs]
    current = coeffs
    for term_index in range(ORDER - 1):
        derived = jnp.einsum("dbc,qce->dbqe", deriv_mats, current, precision=HIGH)
        current = -jnp.sum(
            star_part[:, :, :, None, :] * jnp.swapaxes(derived, 1, 2)[:, None, :, :, :], axis=(0, 2)
        )
        series.append(current)
    return series


def integrate(series, start_time, end_time):
    summed = (end_time - start_time) * series[0]
    for term_index in range(1, len(series)):
        weight = (end_time ** (term_index + 1) - start_time ** (term_index + 1)) / math.factorial(
            term_index + 1
        )
        summed = summed + weight * series[term_index]
    return summed


def series_step(star_part, deriv_mats):
    def step(state):
        current = state[-1]
        derived = jnp.einsum("dbc,qce->dbqe", deriv_mats, current, precision=HIGH)
        following = -jnp.sum(
            star_part[:, :, :, None, :] * jnp.swapaxes(derived, 1, 2)[:, None, :, :, :], axis=(0, 2)
        )
        return state + (following,)

    return step


def weights(start_time, end_time):
    out = [end_time - start_time]
    for term_index in range(1, ORDER):
        out.append(
            (end_time ** (term_index + 1) - start_time ** (term_index + 1))
            / math.factorial(term_index + 1)
        )
    return out


def combine(terms, factors):
    summed = factors[0] * terms[0]
    for term_index in range(1, len(factors)):
        summed = summed + factors[term_index] * terms[term_index]
    return summed


def face_values(integral, face_proj):
    return jnp.einsum("fnb,qbe->qnfe", face_proj, integral, precision=HIGH)


def one_hot(indices, count):
    flat = indices.reshape(-1)
    return (lax.broadcasted_iota(jnp.int32, (count, flat.shape[0]), 0) == flat[None, :]).astype(
        jnp.float32
    )


def pick_columns(values, selector):
    return jnp.einsum("qnc,cx->qnx", values, selector, precision=HIGH)


def route(send_blocks, blocks):
    received = []
    for position in range(2 * REACH):
        offset = position - REACH if position < REACH else position - REACH + 1
        part = send_blocks[:, :, position * blocks : (position + 1) * blocks]
        received.append(passed_along(part, "dom", -offset))
    return jnp.concatenate(received, axis=2)


def face_flux(solver_part, face_data):
    moved = jnp.transpose(face_data, (2, 0, 1, 3))
    return jnp.sum(solver_part[:, :, :, None, :] * moved[:, None, :, :, :], axis=2)


def advance(
    coeffs, integral, own_faces, picked, masks, star_part, volume_mats, face_lift, turned_lift,
    minus_part, plus_part,
):
    starred = jnp.sum(star_part[:, :, :, None, :] * integral[None, None, :, :, :], axis=2)
    gained = jnp.einsum("dbc,dpce->pbe", volume_mats, starred, precision=HIGH)
    own_flux = face_flux(minus_part, own_faces)
    far_flux = face_flux(plus_part, picked)
    masked = masks[:, :, None, None, :] * far_flux[None]
    lifted = jnp.einsum("fbn,fpne->pbe", face_lift, own_flux, precision=HIGH) + jnp.einsum(
        "hfbm,hfpme->pbe", turned_lift, masked, precision=HIGH
    )
    return coeffs + gained - lifted


def local(
    q_state,
    star_mats,
    flux_minus,
    flux_plus,
    time_limit,
    deriv_mats,
    volume_mats,
    face_proj,
    face_lift,
    face_link,
    face_orient,
    send_face,
):
    rotation = rotation_table(face_proj.shape[1])
    inverse = np.argsort(rotation, axis=1)
    turned_lift = jnp.stack([face_lift[:, :, inverse[turn]] for turn in range(3)])
    quantity = q_state.shape[0]
    face_nodes = face_proj.shape[1]
    elem_count = q_state.shape[2]
    face_count = face_link.shape[0]
    own_cols = face_count * elem_count
    blocks = send_face.shape[1]
    fine = FINE_DEV
    send_pick = one_hot(send_face, own_cols)
    send_rows = send_pick.reshape(face_count, elem_count, send_pick.shape[1])
    allowed = jnp.where(jnp.arange(elem_count) < fine, time_limit, time_limit / STEP_RATIO)
    step_fine = global_min(jnp.min(allowed), "dom")
    step_coarse = STEP_RATIO * step_fine
    series = (q_state,)
    for term_index in range(ORDER - 1):
        series = series_step(star_mats, deriv_mats)(series)
    first_weights = weights(0.0, step_fine)
    second_weights = weights(step_fine, step_coarse)
    first = combine(series, first_weights)
    coarse_two = combine([term[:, :, fine:] for term in series], second_weights)
    faces_one = face_values(first, face_proj)
    flat_one = faces_one.reshape(quantity, face_nodes, own_cols)
    received_one = route(pick_columns(flat_one, send_pick), blocks)

    fine_star = star_mats[..., :fine]
    fine_minus = flux_minus[..., :fine]
    fine_plus = flux_plus[..., :fine]
    pool_cols = own_cols + received_one.shape[2]
    masks = jnp.stack([(face_orient == turn).astype(jnp.float32) for turn in range(3)])
    fine_pick = one_hot(face_link[:, :fine], pool_cols)
    picked_one = pick_columns(flat_one, fine_pick[:own_cols]) + pick_columns(
        received_one, fine_pick[own_cols:]
    )
    fine_mid = advance(
        q_state[:, :, :fine],
        first[:, :, :fine],
        faces_one[..., :fine],
        picked_one.reshape(quantity, face_nodes, face_count, fine),
        masks[..., :fine],
        fine_star,
        volume_mats,
        face_lift,
        turned_lift,
        fine_minus,
        fine_plus,
    )
    fine_state = (fine_mid,)
    for term_index in range(ORDER - 1):
        fine_state = series_step(fine_star, deriv_mats)(fine_state)
    fine_two = combine(fine_state, first_weights)
    fine_faces_two = face_values(fine_two, face_proj)
    sends_two = jnp.einsum(
        "qnfe,fes->qns", fine_faces_two, send_rows[:, :fine], precision=HIGH
    )
    coarse_faces_two = face_values(coarse_two, face_proj)
    sends_two = sends_two + jnp.einsum(
        "qnfe,fes->qns", coarse_faces_two, send_rows[:, fine:], precision=HIGH
    )
    received_two = route(sends_two, blocks)
    faces_two = jnp.concatenate([fine_faces_two, coarse_faces_two], axis=3)
    flat_two = faces_two.reshape(quantity, face_nodes, own_cols)

    is_fine = jnp.arange(elem_count) < fine
    all_pick = one_hot(face_link, pool_cols)
    coarse_pick = all_pick * jnp.tile(jnp.logical_not(is_fine), face_count)[None, :].astype(
        jnp.float32
    )
    picked_end = (
        pick_columns(flat_two, all_pick[:own_cols])
        + pick_columns(received_two, all_pick[own_cols:])
        + pick_columns(flat_one, coarse_pick[:own_cols])
        + pick_columns(received_one, coarse_pick[own_cols:])
    )
    own_end = jnp.where(is_fine, faces_two, faces_one + faces_two)
    coeffs_end = jnp.concatenate([fine_mid, q_state[:, :, fine:]], axis=2)
    integral_end = jnp.concatenate([fine_two, first[:, :, fine:] + coarse_two], axis=2)
    return advance(
        coeffs_end,
        integral_end,
        own_end,
        picked_end.reshape(quantity, face_nodes, face_count, elem_count),
        masks,
        star_mats,
        volume_mats,
        face_lift,
        turned_lift,
        flux_minus,
        flux_plus,
    )


def solution(mesh):
    placed = (
        P(None, None, "dom"),
        P(None, None, None, "dom"),
        P(None, None, None, "dom"),
        P(None, None, None, "dom"),
        P("dom"),
        P(),
        P(),
        P(),
        P(),
        P(None, "dom"),
        P(None, "dom"),
        P(None, "dom"),
    )
    return jax.shard_map(
        local, mesh=mesh, in_specs=placed, out_specs=P(None, None, "dom"), check_vma=False
    )
```

```python
import math

import jax
import jax.numpy as jnp
import numpy as np
from jax import lax
from jax.sharding import PartitionSpec as P

ORDER = 6
REACH = 3
FINE_DEV = 64


HIGH = lax.Precision.HIGHEST
STEP_RATIO = 2.0


def passed_along(value, axis, steps):
    count = lax.axis_size(axis)
    leading, last = (max(0, -steps), min(count, count - steps))
    return lax.ppermute(value, axis, [(source, source + steps) for source in range(leading, last)])


def global_min(value, axis):
    count = lax.axis_size(axis)
    if count & (count - 1):
        return lax.pmin(value, axis)
    stride = 1
    while stride < count:
        partner = lax.ppermute(value, axis, [(source, source ^ stride) for source in range(count)])
        value = jnp.minimum(value, partner)
        stride *= 2
    return value


def rotation_table(node_count):
    degree = 0
    while (degree + 1) * (degree + 2) // 2 < node_count:
        degree += 1
    node_pairs = [
        (across, upward) for across in range(degree + 1) for upward in range(degree + 1 - across)
    ]
    lookup = {}
    for number, node_pair in enumerate(node_pairs):
        lookup[node_pair] = number
    tables = []
    for rotations in range(3):
        new_order = []
        for node_pair in node_pairs:
            moved_pair = (node_pair[1], node_pair[0])
            for repeat in range(rotations):
                moved_pair = (moved_pair[1], degree - moved_pair[0] - moved_pair[1])
            new_order.append(lookup[moved_pair])
        tables.append(new_order)
    return np.array(tables, dtype=np.int32)


def taylor_series(coeffs, star_part, deriv_mats):
    series = [coeffs]
    current = coeffs
    for term_index in range(ORDER - 1):
        derived = jnp.einsum("dbc,qce->dbqe", deriv_mats, current, precision=HIGH)
        current = -jnp.sum(
            star_part[:, :, :, None, :] * jnp.swapaxes(derived, 1, 2)[:, None, :, :, :], axis=(0, 2)
        )
        series.append(current)
    return series


def integrate(series, start_time, end_time):
    summed = (end_time - start_time) * series[0]
    for term_index in range(1, len(series)):
        weight = (end_time ** (term_index + 1) - start_time ** (term_index + 1)) / math.factorial(
            term_index + 1
        )
        summed = summed + weight * series[term_index]
    return summed


def series_step(star_part, deriv_mats):
    def step(state):
        current = state[-1]
        derived = jnp.einsum("dbc,qce->dbqe", deriv_mats, current, precision=HIGH)
        following = -jnp.sum(
            star_part[:, :, :, None, :] * jnp.swapaxes(derived, 1, 2)[:, None, :, :, :], axis=(0, 2)
        )
        return state + (following,)

    return step


def weights(start_time, end_time):
    out = [end_time - start_time]
    for term_index in range(1, ORDER):
        out.append(
            (end_time ** (term_index + 1) - start_time ** (term_index + 1))
            / math.factorial(term_index + 1)
        )
    return out


def combine(terms, factors):
    summed = factors[0] * terms[0]
    for term_index in range(1, len(factors)):
        summed = summed + factors[term_index] * terms[term_index]
    return summed


def face_values(integral, face_proj):
    return jnp.einsum("fnb,qbe->qnfe", face_proj, integral, precision=HIGH)


def one_hot(indices, count):
    flat = indices.reshape(-1)
    return (lax.broadcasted_iota(jnp.int32, (count, flat.shape[0]), 0) == flat[None, :]).astype(
        jnp.float32
    )


def pick_columns(values, selector):
    return jnp.einsum("qnc,cx->qnx", values, selector, precision=HIGH)


def route(send_blocks, blocks):
    received = []
    for position in range(2 * REACH):
        offset = position - REACH if position < REACH else position - REACH + 1
        part = send_blocks[:, :, position * blocks : (position + 1) * blocks]
        received.append(passed_along(part, "dom", -offset))
    return received


def face_flux(solver_part, face_data):
    moved = jnp.transpose(face_data, (2, 0, 1, 3))
    return jnp.sum(solver_part[:, :, :, None, :] * moved[:, None, :, :, :], axis=2)


def lift_far(picked, masks, turned_lift, plus_part):
    far_flux = face_flux(plus_part, picked)
    masked = masks[:, :, None, None, :] * far_flux[None]
    return jnp.einsum("hfbm,hfpme->pbe", turned_lift, masked, precision=HIGH)


def advance(
    coeffs, integral, own_faces, picked, masks, star_part, volume_mats, face_lift, turned_lift,
    minus_part, plus_part,
):
    starred = jnp.sum(star_part[:, :, :, None, :] * integral[None, None, :, :, :], axis=2)
    gained = jnp.einsum("dbc,dpce->pbe", volume_mats, starred, precision=HIGH)
    own_flux = face_flux(minus_part, own_faces)
    lifted = jnp.einsum("fbn,fpne->pbe", face_lift, own_flux, precision=HIGH)
    return coeffs + gained - lifted - lift_far(picked, masks, turned_lift, plus_part)


def pick_blocks(blocks_in, selector, own_cols):
    size = blocks_in[0].shape[2]
    summed = None
    for position, block in enumerate(blocks_in):
        start = own_cols + position * size
        part = pick_columns(block, selector[start : start + size])
        summed = part if summed is None else summed + part
    return summed


def local(
    q_state,
    star_mats,
    flux_minus,
    flux_plus,
    time_limit,
    deriv_mats,
    volume_mats,
    face_proj,
    face_lift,
    face_link,
    face_orient,
    send_face,
):
    rotation = rotation_table(face_proj.shape[1])
    inverse = np.argsort(rotation, axis=1)
    turned_lift = jnp.stack([face_lift[:, :, inverse[turn]] for turn in range(3)])
    quantity = q_state.shape[0]
    face_nodes = face_proj.shape[1]
    elem_count = q_state.shape[2]
    face_count = face_link.shape[0]
    own_cols = face_count * elem_count
    blocks = send_face.shape[1]
    fine = FINE_DEV
    send_pick = one_hot(send_face, own_cols)
    send_rows = send_pick.reshape(face_count, elem_count, send_pick.shape[1])
    allowed = jnp.where(jnp.arange(elem_count) < fine, time_limit, time_limit / STEP_RATIO)
    step_fine = global_min(jnp.min(allowed), "dom")
    step_coarse = STEP_RATIO * step_fine
    series = (q_state,)
    for term_index in range(ORDER - 1):
        series = series_step(star_mats, deriv_mats)(series)
    first_weights = weights(0.0, step_fine)
    second_weights = weights(step_fine, step_coarse)
    first = combine(series, first_weights)
    coarse_two = combine([term[:, :, fine:] for term in series], second_weights)
    faces_one = face_values(first, face_proj)
    flat_one = faces_one.reshape(quantity, face_nodes, own_cols)
    received_one = route(pick_columns(flat_one, send_pick), blocks)

    fine_star = star_mats[..., :fine]
    fine_minus = flux_minus[..., :fine]
    fine_plus = flux_plus[..., :fine]
    pool_cols = own_cols + blocks * len(received_one)
    masks = jnp.stack([(face_orient == turn).astype(jnp.float32) for turn in range(3)])
    fine_pick = one_hot(face_link[:, :fine], pool_cols)
    picked_one = pick_columns(flat_one, fine_pick[:own_cols])
    far_one = pick_blocks(received_one, fine_pick, own_cols)
    fine_mid = advance(
        q_state[:, :, :fine],
        first[:, :, :fine],
        faces_one[..., :fine],
        picked_one.reshape(quantity, face_nodes, face_count, fine),
        masks[..., :fine],
        fine_star,
        volume_mats,
        face_lift,
        turned_lift,
        fine_minus,
        fine_plus,
    ) - lift_far(
        far_one.reshape(quantity, face_nodes, face_count, fine), masks[..., :fine], turned_lift, fine_plus
    )
    fine_state = (fine_mid,)
    for term_index in range(ORDER - 1):
        fine_state = series_step(fine_star, deriv_mats)(fine_state)
    fine_two = combine(fine_state, first_weights)
    fine_faces_two = face_values(fine_two, face_proj)
    sends_two = jnp.einsum(
        "qnfe,fes->qns", fine_faces_two, send_rows[:, :fine], precision=HIGH
    )
    coarse_faces_two = face_values(coarse_two, face_proj)
    sends_two = sends_two + jnp.einsum(
        "qnfe,fes->qns", coarse_faces_two, send_rows[:, fine:], precision=HIGH
    )
    received_two = route(sends_two, blocks)
    faces_two = jnp.concatenate([fine_faces_two, coarse_faces_two], axis=3)
    flat_two = faces_two.reshape(quantity, face_nodes, own_cols)

    is_fine = jnp.arange(elem_count) < fine
    all_pick = one_hot(face_link, pool_cols)
    coarse_pick = all_pick * jnp.tile(jnp.logical_not(is_fine), face_count)[None, :].astype(
        jnp.float32
    )
    picked_end = (
        pick_columns(flat_two, all_pick[:own_cols])
        + pick_columns(flat_one, coarse_pick[:own_cols])
        + pick_blocks(received_one, coarse_pick, own_cols)
    )
    far_end = pick_blocks(received_two, all_pick, own_cols)
    own_end = jnp.where(is_fine, faces_two, faces_one + faces_two)
    coeffs_end = jnp.concatenate([fine_mid, q_state[:, :, fine:]], axis=2)
    integral_end = jnp.concatenate([fine_two, first[:, :, fine:] + coarse_two], axis=2)
    return advance(
        coeffs_end,
        integral_end,
        own_end,
        picked_end.reshape(quantity, face_nodes, face_count, elem_count),
        masks,
        star_mats,
        volume_mats,
        face_lift,
        turned_lift,
        flux_minus,
        flux_plus,
    ) - lift_far(
        far_end.reshape(quantity, face_nodes, face_count, elem_count), masks, turned_lift, flux_plus
    )


def solution(mesh):
    placed = (
        P(None, None, "dom"),
        P(None, None, None, "dom"),
        P(None, None, None, "dom"),
        P(None, None, None, "dom"),
        P("dom"),
        P(),
        P(),
        P(),
        P(),
        P(None, "dom"),
        P(None, "dom"),
        P(None, "dom"),
    )
    return jax.shard_map(
        local, mesh=mesh, in_specs=placed, out_specs=P(None, None, "dom"), check_vma=False
    )
```

```python
import math

import jax
import jax.numpy as jnp
import numpy as np
from jax import lax
from jax.sharding import PartitionSpec as P

ORDER = 6
REACH = 3
FINE_DEV = 64


HIGH = lax.Precision.HIGHEST
STEP_RATIO = 2.0


def passed_along(value, axis, steps):
    count = lax.axis_size(axis)
    leading, last = (max(0, -steps), min(count, count - steps))
    return lax.ppermute(value, axis, [(source, source + steps) for source in range(leading, last)])


def global_min(value, axis):
    count = lax.axis_size(axis)
    if count & (count - 1):
        return lax.pmin(value, axis)
    stride = 1
    while stride < count:
        partner = lax.ppermute(value, axis, [(source, source ^ stride) for source in range(count)])
        value = jnp.minimum(value, partner)
        stride *= 2
    return value


def rotation_table(node_count):
    degree = 0
    while (degree + 1) * (degree + 2) // 2 < node_count:
        degree += 1
    node_pairs = [
        (across, upward) for across in range(degree + 1) for upward in range(degree + 1 - across)
    ]
    lookup = {}
    for number, node_pair in enumerate(node_pairs):
        lookup[node_pair] = number
    tables = []
    for rotations in range(3):
        new_order = []
        for node_pair in node_pairs:
            moved_pair = (node_pair[1], node_pair[0])
            for repeat in range(rotations):
                moved_pair = (moved_pair[1], degree - moved_pair[0] - moved_pair[1])
            new_order.append(lookup[moved_pair])
        tables.append(new_order)
    return np.array(tables, dtype=np.int32)


def taylor_series(coeffs, star_part, deriv_mats):
    series = [coeffs]
    current = coeffs
    for term_index in range(ORDER - 1):
        derived = jnp.einsum("dbc,qce->dbqe", deriv_mats, current, precision=HIGH)
        current = -jnp.sum(
            star_part[:, :, :, None, :] * jnp.swapaxes(derived, 1, 2)[:, None, :, :, :], axis=(0, 2)
        )
        series.append(current)
    return series


def integrate(series, start_time, end_time):
    summed = (end_time - start_time) * series[0]
    for term_index in range(1, len(series)):
        weight = (end_time ** (term_index + 1) - start_time ** (term_index + 1)) / math.factorial(
            term_index + 1
        )
        summed = summed + weight * series[term_index]
    return summed


def series_step(star_part, deriv_mats):
    def step(state):
        current = state[-1]
        derived = jnp.einsum("dbc,qce->dbqe", deriv_mats, current, precision=HIGH)
        following = -jnp.sum(
            star_part[:, :, :, None, :] * jnp.swapaxes(derived, 1, 2)[:, None, :, :, :], axis=(0, 2)
        )
        return state + (following,)

    return step


def weights(start_time, end_time):
    out = [end_time - start_time]
    for term_index in range(1, ORDER):
        out.append(
            (end_time ** (term_index + 1) - start_time ** (term_index + 1))
            / math.factorial(term_index + 1)
        )
    return out


def combine(terms, factors):
    summed = factors[0] * terms[0]
    for term_index in range(1, len(factors)):
        summed = summed + factors[term_index] * terms[term_index]
    return summed


def face_values(integral, face_proj):
    return jnp.einsum("fnb,qbe->qnfe", face_proj, integral, precision=HIGH)


def one_hot(indices, count):
    flat = indices.reshape(-1)
    return (lax.broadcasted_iota(jnp.int32, (count, flat.shape[0]), 0) == flat[None, :]).astype(
        jnp.float32
    )


def pick_columns(values, selector):
    return jnp.einsum("qnc,cx->qnx", values, selector, precision=HIGH)


def slot_gather(integral, selector):
    return jnp.einsum("qbe,eks->kqbs", integral, selector, precision=HIGH)


def slot_faces(gathered, face_proj, face_sel):
    face_count, face_nodes = face_proj.shape[:2]
    rows = face_proj.reshape(face_count * face_nodes, face_proj.shape[2])
    projected = jnp.einsum("xb,kqbs->kqxs", rows, gathered, precision=HIGH)
    summed = None
    for face in range(face_count):
        part = face_sel[face][:, None, None, :] * projected[:, :, face * face_nodes : (face + 1) * face_nodes, :]
        summed = part if summed is None else summed + part
    return summed


def route(send_blocks, blocks):
    received = []
    for position in range(2 * REACH):
        offset = position - REACH if position < REACH else position - REACH + 1
        part = send_blocks[position]
        received.append(passed_along(part, "dom", -offset))
    return jnp.concatenate(received, axis=2)


def face_flux(solver_part, face_data):
    moved = jnp.transpose(face_data, (2, 0, 1, 3))
    return jnp.sum(solver_part[:, :, :, None, :] * moved[:, None, :, :, :], axis=2)


def advance(
    coeffs, integral, own_faces, picked, masks, star_part, volume_mats, face_lift, turned_lift,
    minus_part, plus_part,
):
    starred = jnp.sum(star_part[:, :, :, None, :] * integral[None, None, :, :, :], axis=2)
    gained = jnp.einsum("dbc,dpce->pbe", volume_mats, starred, precision=HIGH)
    own_flux = face_flux(minus_part, own_faces)
    far_flux = face_flux(plus_part, picked)
    masked = masks[:, :, None, None, :] * far_flux[None]
    lifted = jnp.einsum("fbn,fpne->pbe", face_lift, own_flux, precision=HIGH) + jnp.einsum(
        "hfbm,hfpme->pbe", turned_lift, masked, precision=HIGH
    )
    return coeffs + gained - lifted


def local(
    q_state,
    star_mats,
    flux_minus,
    flux_plus,
    time_limit,
    deriv_mats,
    volume_mats,
    face_proj,
    face_lift,
    face_link,
    face_orient,
    send_face,
):
    rotation = rotation_table(face_proj.shape[1])
    inverse = np.argsort(rotation, axis=1)
    turned_lift = jnp.stack([face_lift[:, :, inverse[turn]] for turn in range(3)])
    quantity = q_state.shape[0]
    face_nodes = face_proj.shape[1]
    elem_count = q_state.shape[2]
    face_count = face_link.shape[0]
    own_cols = face_count * elem_count
    blocks = send_face.shape[1]
    fine = FINE_DEV
    slot_elem = (
        lax.broadcasted_iota(jnp.int32, (elem_count,) + send_face.shape, 0) == (send_face % elem_count)[None]
    ).astype(jnp.float32)
    slot_face = (
        lax.broadcasted_iota(jnp.int32, (face_count,) + send_face.shape, 0) == (send_face // elem_count)[None]
    ).astype(jnp.float32) * (send_face >= 0)[None].astype(jnp.float32)
    allowed = jnp.where(jnp.arange(elem_count) < fine, time_limit, time_limit / STEP_RATIO)
    step_fine = global_min(jnp.min(allowed), "dom")
    step_coarse = STEP_RATIO * step_fine
    series = (q_state,)
    for term_index in range(ORDER - 1):
        series = series_step(star_mats, deriv_mats)(series)
    first_weights = weights(0.0, step_fine)
    second_weights = weights(step_fine, step_coarse)
    first = combine(series, first_weights)
    coarse_two = combine([term[:, :, fine:] for term in series], second_weights)
    faces_one = face_values(first, face_proj)
    flat_one = faces_one.reshape(quantity, face_nodes, own_cols)
    received_one = route(slot_faces(slot_gather(first, slot_elem), face_proj, slot_face), blocks)

    fine_star = star_mats[..., :fine]
    fine_minus = flux_minus[..., :fine]
    fine_plus = flux_plus[..., :fine]
    pool_cols = own_cols + received_one.shape[2]
    masks = jnp.stack([(face_orient == turn).astype(jnp.float32) for turn in range(3)])
    fine_pick = one_hot(face_link[:, :fine], pool_cols)
    picked_one = pick_columns(flat_one, fine_pick[:own_cols]) + pick_columns(
        received_one, fine_pick[own_cols:]
    )
    fine_mid = advance(
        q_state[:, :, :fine],
        first[:, :, :fine],
        faces_one[..., :fine],
        picked_one.reshape(quantity, face_nodes, face_count, fine),
        masks[..., :fine],
        fine_star,
        volume_mats,
        face_lift,
        turned_lift,
        fine_minus,
        fine_plus,
    )
    fine_state = (fine_mid,)
    for term_index in range(ORDER - 1):
        fine_state = series_step(fine_star, deriv_mats)(fine_state)
    fine_two = combine(fine_state, first_weights)
    gathered_two = slot_gather(fine_two, slot_elem[:fine]) + slot_gather(coarse_two, slot_elem[fine:])
    sends_two = slot_faces(gathered_two, face_proj, slot_face)
    fine_faces_two = face_values(fine_two, face_proj)
    coarse_faces_two = face_values(coarse_two, face_proj)
    received_two = route(sends_two, blocks)
    faces_two = jnp.concatenate([fine_faces_two, coarse_faces_two], axis=3)
    flat_two = faces_two.reshape(quantity, face_nodes, own_cols)

    is_fine = jnp.arange(elem_count) < fine
    all_pick = one_hot(face_link, pool_cols)
    coarse_pick = all_pick * jnp.tile(jnp.logical_not(is_fine), face_count)[None, :].astype(
        jnp.float32
    )
    picked_end = (
        pick_columns(flat_two, all_pick[:own_cols])
        + pick_columns(received_two, all_pick[own_cols:])
        + pick_columns(flat_one, coarse_pick[:own_cols])
        + pick_columns(received_one, coarse_pick[own_cols:])
    )
    own_end = jnp.where(is_fine, faces_two, faces_one + faces_two)
    coeffs_end = jnp.concatenate([fine_mid, q_state[:, :, fine:]], axis=2)
    integral_end = jnp.concatenate([fine_two, first[:, :, fine:] + coarse_two], axis=2)
    return advance(
        coeffs_end,
        integral_end,
        own_end,
        picked_end.reshape(quantity, face_nodes, face_count, elem_count),
        masks,
        star_mats,
        volume_mats,
        face_lift,
        turned_lift,
        flux_minus,
        flux_plus,
    )


def solution(mesh):
    placed = (
        P(None, None, "dom"),
        P(None, None, None, "dom"),
        P(None, None, None, "dom"),
        P(None, None, None, "dom"),
        P("dom"),
        P(),
        P(),
        P(),
        P(),
        P(None, "dom"),
        P(None, "dom"),
        P(None, "dom"),
    )
    return jax.shard_map(
        local, mesh=mesh, in_specs=placed, out_specs=P(None, None, "dom"), check_vma=False
    )
```

```python
import math

import jax
import jax.numpy as jnp
import numpy as np
from jax import lax
from jax.sharding import PartitionSpec as P

ORDER = 6
REACH = 3
FINE_DEV = 64


HIGH = lax.Precision.HIGHEST
STEP_RATIO = 2.0


def passed_along(value, axis, steps):
    count = lax.axis_size(axis)
    leading, last = (max(0, -steps), min(count, count - steps))
    return lax.ppermute(value, axis, [(source, source + steps) for source in range(leading, last)])


def global_min(value, axis):
    count = lax.axis_size(axis)
    if count & (count - 1):
        return lax.pmin(value, axis)
    stride = 1
    while stride < count:
        partner = lax.ppermute(value, axis, [(source, source ^ stride) for source in range(count)])
        value = jnp.minimum(value, partner)
        stride *= 2
    return value


def rotation_table(node_count):
    degree = 0
    while (degree + 1) * (degree + 2) // 2 < node_count:
        degree += 1
    node_pairs = [
        (across, upward) for across in range(degree + 1) for upward in range(degree + 1 - across)
    ]
    lookup = {}
    for number, node_pair in enumerate(node_pairs):
        lookup[node_pair] = number
    tables = []
    for rotations in range(3):
        new_order = []
        for node_pair in node_pairs:
            moved_pair = (node_pair[1], node_pair[0])
            for repeat in range(rotations):
                moved_pair = (moved_pair[1], degree - moved_pair[0] - moved_pair[1])
            new_order.append(lookup[moved_pair])
        tables.append(new_order)
    return np.array(tables, dtype=np.int32)


def taylor_series(coeffs, star_part, deriv_mats):
    series = [coeffs]
    current = coeffs
    for term_index in range(ORDER - 1):
        derived = jnp.einsum("dbc,qce->dbqe", deriv_mats, current, precision=HIGH)
        current = -jnp.sum(
            star_part[:, :, :, None, :] * jnp.swapaxes(derived, 1, 2)[:, None, :, :, :], axis=(0, 2)
        )
        series.append(current)
    return series


def integrate(series, start_time, end_time):
    summed = (end_time - start_time) * series[0]
    for term_index in range(1, len(series)):
        weight = (end_time ** (term_index + 1) - start_time ** (term_index + 1)) / math.factorial(
            term_index + 1
        )
        summed = summed + weight * series[term_index]
    return summed


def series_step(star_part, deriv_mats):
    def step(state):
        current = state[-1]
        derived = jnp.einsum("dbc,qce->dbqe", deriv_mats, current, precision=HIGH)
        following = -jnp.sum(
            star_part[:, :, :, None, :] * jnp.swapaxes(derived, 1, 2)[:, None, :, :, :], axis=(0, 2)
        )
        return state + (following,)

    return step


def weights(start_time, end_time):
    out = [end_time - start_time]
    for term_index in range(1, ORDER):
        out.append(
            (end_time ** (term_index + 1) - start_time ** (term_index + 1))
            / math.factorial(term_index + 1)
        )
    return out


def combine(terms, factors):
    summed = factors[0] * terms[0]
    for term_index in range(1, len(factors)):
        summed = summed + factors[term_index] * terms[term_index]
    return summed


def face_values(integral, face_proj):
    return jnp.einsum("fnb,qbe->qnfe", face_proj, integral, precision=HIGH)


def one_hot(indices, count):
    flat = indices.reshape(-1)
    return (lax.broadcasted_iota(jnp.int32, (count, flat.shape[0]), 0) == flat[None, :]).astype(
        jnp.float32
    )


def pick_columns(values, selector):
    return jnp.einsum("qnc,cx->qnx", values, selector, precision=HIGH)


def route(send_blocks, blocks):
    received = []
    for position in range(2 * REACH):
        offset = position - REACH if position < REACH else position - REACH + 1
        part = send_blocks[:, :, position * blocks : (position + 1) * blocks]
        received.append(passed_along(part, "dom", -offset))
    return jnp.concatenate(received, axis=2)


def face_flux(solver_part, face_data):
    moved = jnp.transpose(face_data, (2, 0, 1, 3))
    return jnp.sum(solver_part[:, :, :, None, :] * moved[:, None, :, :, :], axis=2)


def advance(
    coeffs, integral, own_faces, picked, masks, star_part, volume_mats, face_lift, turned_lift,
    minus_part, plus_part,
):
    starred = jnp.sum(star_part[:, :, :, None, :] * integral[None, None, :, :, :], axis=2)
    gained = jnp.einsum("dbc,dpce->pbe", volume_mats, starred, precision=HIGH)
    own_flux = face_flux(minus_part, own_faces)
    far_flux = face_flux(plus_part, picked)
    masked = masks[:, :, None, None, :] * far_flux[None]
    lifted = jnp.einsum("fbn,fpne->pbe", face_lift, own_flux, precision=HIGH) + jnp.einsum(
        "hfbm,hfpme->pbe", turned_lift, masked, precision=HIGH
    )
    return coeffs + gained - lifted


def local(
    q_state,
    star_mats,
    flux_minus,
    flux_plus,
    time_limit,
    deriv_mats,
    volume_mats,
    face_proj,
    face_lift,
    face_link,
    face_orient,
    send_face,
):
    rotation = rotation_table(face_proj.shape[1])
    inverse = np.argsort(rotation, axis=1)
    turned_lift = jnp.stack([face_lift[:, :, inverse[turn]] for turn in range(3)])
    quantity = q_state.shape[0]
    face_nodes = face_proj.shape[1]
    elem_count = q_state.shape[2]
    face_count = face_link.shape[0]
    own_cols = face_count * elem_count
    blocks = send_face.shape[1]
    fine = FINE_DEV
    send_pick = one_hot(send_face, own_cols)
    send_rows = send_pick.reshape(face_count, elem_count, send_pick.shape[1])
    allowed = jnp.where(jnp.arange(elem_count) < fine, time_limit, time_limit / STEP_RATIO)
    step_fine = global_min(jnp.min(allowed), "dom")
    step_coarse = STEP_RATIO * step_fine
    def scan_step(current, unused):
        following = series_step(star_mats, deriv_mats)((current,))[-1]
        return following, following

    scanned = lax.scan(scan_step, q_state, None, length=ORDER - 1)[1]
    series = (q_state,) + tuple(scanned[term_index] for term_index in range(ORDER - 1))
    first_weights = weights(0.0, step_fine)
    second_weights = weights(step_fine, step_coarse)
    first = combine(series, first_weights)
    coarse_two = combine([term[:, :, fine:] for term in series], second_weights)
    faces_one = face_values(first, face_proj)
    flat_one = faces_one.reshape(quantity, face_nodes, own_cols)
    received_one = route(pick_columns(flat_one, send_pick), blocks)

    fine_star = star_mats[..., :fine]
    fine_minus = flux_minus[..., :fine]
    fine_plus = flux_plus[..., :fine]
    pool_cols = own_cols + received_one.shape[2]
    masks = jnp.stack([(face_orient == turn).astype(jnp.float32) for turn in range(3)])
    fine_pick = one_hot(face_link[:, :fine], pool_cols)
    picked_one = pick_columns(flat_one, fine_pick[:own_cols]) + pick_columns(
        received_one, fine_pick[own_cols:]
    )
    fine_mid = advance(
        q_state[:, :, :fine],
        first[:, :, :fine],
        faces_one[..., :fine],
        picked_one.reshape(quantity, face_nodes, face_count, fine),
        masks[..., :fine],
        fine_star,
        volume_mats,
        face_lift,
        turned_lift,
        fine_minus,
        fine_plus,
    )
    fine_state = (fine_mid,)
    for term_index in range(ORDER - 1):
        fine_state = series_step(fine_star, deriv_mats)(fine_state)
    fine_two = combine(fine_state, first_weights)
    fine_faces_two = face_values(fine_two, face_proj)
    sends_two = jnp.einsum(
        "qnfe,fes->qns", fine_faces_two, send_rows[:, :fine], precision=HIGH
    )
    coarse_faces_two = face_values(coarse_two, face_proj)
    sends_two = sends_two + jnp.einsum(
        "qnfe,fes->qns", coarse_faces_two, send_rows[:, fine:], precision=HIGH
    )
    received_two = route(sends_two, blocks)
    faces_two = jnp.concatenate([fine_faces_two, coarse_faces_two], axis=3)
    flat_two = faces_two.reshape(quantity, face_nodes, own_cols)

    is_fine = jnp.arange(elem_count) < fine
    all_pick = one_hot(face_link, pool_cols)
    coarse_pick = all_pick * jnp.tile(jnp.logical_not(is_fine), face_count)[None, :].astype(
        jnp.float32
    )
    picked_end = (
        pick_columns(flat_two, all_pick[:own_cols])
        + pick_columns(received_two, all_pick[own_cols:])
        + pick_columns(flat_one, coarse_pick[:own_cols])
        + pick_columns(received_one, coarse_pick[own_cols:])
    )
    own_end = jnp.where(is_fine, faces_two, faces_one + faces_two)
    coeffs_end = jnp.concatenate([fine_mid, q_state[:, :, fine:]], axis=2)
    integral_end = jnp.concatenate([fine_two, first[:, :, fine:] + coarse_two], axis=2)
    return advance(
        coeffs_end,
        integral_end,
        own_end,
        picked_end.reshape(quantity, face_nodes, face_count, elem_count),
        masks,
        star_mats,
        volume_mats,
        face_lift,
        turned_lift,
        flux_minus,
        flux_plus,
    )


def solution(mesh):
    placed = (
        P(None, None, "dom"),
        P(None, None, None, "dom"),
        P(None, None, None, "dom"),
        P(None, None, None, "dom"),
        P("dom"),
        P(),
        P(),
        P(),
        P(),
        P(None, "dom"),
        P(None, "dom"),
        P(None, "dom"),
    )
    return jax.shard_map(
        local, mesh=mesh, in_specs=placed, out_specs=P(None, None, "dom"), check_vma=False
    )
```

```python
import math

import jax
import jax.numpy as jnp
import numpy as np
from jax import lax
from jax.sharding import PartitionSpec as P

ORDER = 6
REACH = 3
FINE_DEV = 64


HIGH = lax.Precision.HIGHEST
STEP_RATIO = 2.0


def passed_along(value, axis, steps):
    count = lax.axis_size(axis)
    leading, last = (max(0, -steps), min(count, count - steps))
    return lax.ppermute(value, axis, [(source, source + steps) for source in range(leading, last)])


def global_min(value, axis):
    count = lax.axis_size(axis)
    if count & (count - 1):
        return lax.pmin(value, axis)
    stride = count // 2
    while stride >= 1:
        partner = lax.ppermute(value, axis, [(source, source ^ stride) for source in range(count)])
        value = jnp.minimum(value, partner)
        stride //= 2
    return value


def rotation_table(node_count):
    degree = 0
    while (degree + 1) * (degree + 2) // 2 < node_count:
        degree += 1
    node_pairs = [
        (across, upward) for across in range(degree + 1) for upward in range(degree + 1 - across)
    ]
    lookup = {}
    for number, node_pair in enumerate(node_pairs):
        lookup[node_pair] = number
    tables = []
    for rotations in range(3):
        new_order = []
        for node_pair in node_pairs:
            moved_pair = (node_pair[1], node_pair[0])
            for repeat in range(rotations):
                moved_pair = (moved_pair[1], degree - moved_pair[0] - moved_pair[1])
            new_order.append(lookup[moved_pair])
        tables.append(new_order)
    return np.array(tables, dtype=np.int32)


def taylor_series(coeffs, star_part, deriv_mats):
    series = [coeffs]
    current = coeffs
    for term_index in range(ORDER - 1):
        derived = jnp.einsum("dbc,qce->dbqe", deriv_mats, current, precision=HIGH)
        current = -jnp.sum(
            star_part[:, :, :, None, :] * jnp.swapaxes(derived, 1, 2)[:, None, :, :, :], axis=(0, 2)
        )
        series.append(current)
    return series


def integrate(series, start_time, end_time):
    summed = (end_time - start_time) * series[0]
    for term_index in range(1, len(series)):
        weight = (end_time ** (term_index + 1) - start_time ** (term_index + 1)) / math.factorial(
            term_index + 1
        )
        summed = summed + weight * series[term_index]
    return summed


def series_step(star_part, deriv_mats):
    def step(state):
        current = state[-1]
        derived = jnp.einsum("dbc,qce->dbqe", deriv_mats, current, precision=HIGH)
        following = -jnp.sum(
            star_part[:, :, :, None, :] * jnp.swapaxes(derived, 1, 2)[:, None, :, :, :], axis=(0, 2)
        )
        return state + (following,)

    return step


def weights(start_time, end_time):
    out = [end_time - start_time]
    for term_index in range(1, ORDER):
        out.append(
            (end_time ** (term_index + 1) - start_time ** (term_index + 1))
            / math.factorial(term_index + 1)
        )
    return out


def combine(terms, factors):
    summed = factors[0] * terms[0]
    for term_index in range(1, len(factors)):
        summed = summed + factors[term_index] * terms[term_index]
    return summed


def face_values(integral, face_proj):
    return jnp.einsum("fnb,qbe->qnfe", face_proj, integral, precision=HIGH)


def one_hot(indices, count):
    flat = indices.reshape(-1)
    return (lax.broadcasted_iota(jnp.int32, (count, flat.shape[0]), 0) == flat[None, :]).astype(
        jnp.float32
    )


def pick_columns(values, selector):
    return jnp.einsum("qnc,cx->qnx", values, selector, precision=HIGH)


def route(send_blocks, blocks):
    received = []
    for position in range(2 * REACH):
        offset = position - REACH if position < REACH else position - REACH + 1
        part = send_blocks[:, :, position * blocks : (position + 1) * blocks]
        received.append(passed_along(part, "dom", -offset))
    return jnp.concatenate(received, axis=2)


def face_flux(solver_part, face_data):
    moved = jnp.transpose(face_data, (2, 0, 1, 3))
    return jnp.sum(solver_part[:, :, :, None, :] * moved[:, None, :, :, :], axis=2)


def advance(
    coeffs, integral, own_faces, picked, masks, star_part, volume_mats, face_lift, turned_lift,
    minus_part, plus_part,
):
    starred = jnp.sum(star_part[:, :, :, None, :] * integral[None, None, :, :, :], axis=2)
    gained = jnp.einsum("dbc,dpce->pbe", volume_mats, starred, precision=HIGH)
    own_flux = face_flux(minus_part, own_faces)
    far_flux = face_flux(plus_part, picked)
    masked = masks[:, :, None, None, :] * far_flux[None]
    lifted = jnp.einsum("fbn,fpne->pbe", face_lift, own_flux, precision=HIGH) + jnp.einsum(
        "hfbm,hfpme->pbe", turned_lift, masked, precision=HIGH
    )
    return coeffs + gained - lifted


def local(
    q_state,
    star_mats,
    flux_minus,
    flux_plus,
    time_limit,
    deriv_mats,
    volume_mats,
    face_proj,
    face_lift,
    face_link,
    face_orient,
    send_face,
):
    rotation = rotation_table(face_proj.shape[1])
    inverse = np.argsort(rotation, axis=1)
    turned_lift = jnp.stack([face_lift[:, :, inverse[turn]] for turn in range(3)])
    quantity = q_state.shape[0]
    face_nodes = face_proj.shape[1]
    elem_count = q_state.shape[2]
    face_count = face_link.shape[0]
    own_cols = face_count * elem_count
    blocks = send_face.shape[1]
    fine = FINE_DEV
    send_pick = one_hot(send_face, own_cols)
    send_rows = send_pick.reshape(face_count, elem_count, send_pick.shape[1])
    allowed = jnp.where(jnp.arange(elem_count) < fine, time_limit, time_limit / STEP_RATIO)
    step_fine = global_min(jnp.min(allowed), "dom")
    step_coarse = STEP_RATIO * step_fine
    series = (q_state,)
    for term_index in range(ORDER - 1):
        series = series_step(star_mats, deriv_mats)(series)
    first_weights = weights(0.0, step_fine)
    second_weights = weights(step_fine, step_coarse)
    first = combine(series, first_weights)
    coarse_two = combine([term[:, :, fine:] for term in series], second_weights)
    faces_one = face_values(first, face_proj)
    flat_one = faces_one.reshape(quantity, face_nodes, own_cols)
    received_one = route(pick_columns(flat_one, send_pick), blocks)

    fine_star = star_mats[..., :fine]
    fine_minus = flux_minus[..., :fine]
    fine_plus = flux_plus[..., :fine]
    pool_cols = own_cols + received_one.shape[2]
    masks = jnp.stack([(face_orient == turn).astype(jnp.float32) for turn in range(3)])
    fine_pick = one_hot(face_link[:, :fine], pool_cols)
    picked_one = pick_columns(flat_one, fine_pick[:own_cols]) + pick_columns(
        received_one, fine_pick[own_cols:]
    )
    fine_mid = advance(
        q_state[:, :, :fine],
        first[:, :, :fine],
        faces_one[..., :fine],
        picked_one.reshape(quantity, face_nodes, face_count, fine),
        masks[..., :fine],
        fine_star,
        volume_mats,
        face_lift,
        turned_lift,
        fine_minus,
        fine_plus,
    )
    fine_state = (fine_mid,)
    for term_index in range(ORDER - 1):
        fine_state = series_step(fine_star, deriv_mats)(fine_state)
    fine_two = combine(fine_state, first_weights)
    fine_faces_two = face_values(fine_two, face_proj)
    sends_two = jnp.einsum(
        "qnfe,fes->qns", fine_faces_two, send_rows[:, :fine], precision=HIGH
    )
    coarse_faces_two = face_values(coarse_two, face_proj)
    sends_two = sends_two + jnp.einsum(
        "qnfe,fes->qns", coarse_faces_two, send_rows[:, fine:], precision=HIGH
    )
    received_two = route(sends_two, blocks)
    faces_two = jnp.concatenate([fine_faces_two, coarse_faces_two], axis=3)
    flat_two = faces_two.reshape(quantity, face_nodes, own_cols)

    is_fine = jnp.arange(elem_count) < fine
    all_pick = one_hot(face_link, pool_cols)
    coarse_pick = one_hot(jnp.where(is_fine[None, :], -1, face_link), pool_cols)
    picked_end = (
        pick_columns(flat_two, all_pick[:own_cols])
        + pick_columns(received_two, all_pick[own_cols:])
        + pick_columns(flat_one, coarse_pick[:own_cols])
        + pick_columns(received_one, coarse_pick[own_cols:])
    )
    own_end = jnp.where(is_fine, faces_two, faces_one + faces_two)
    coeffs_end = jnp.concatenate([fine_mid, q_state[:, :, fine:]], axis=2)
    integral_end = jnp.concatenate([fine_two, first[:, :, fine:] + coarse_two], axis=2)
    return advance(
        coeffs_end,
        integral_end,
        own_end,
        picked_end.reshape(quantity, face_nodes, face_count, elem_count),
        masks,
        star_mats,
        volume_mats,
        face_lift,
        turned_lift,
        flux_minus,
        flux_plus,
    )


def solution(mesh):
    placed = (
        P(None, None, "dom"),
        P(None, None, None, "dom"),
        P(None, None, None, "dom"),
        P(None, None, None, "dom"),
        P("dom"),
        P(),
        P(),
        P(),
        P(),
        P(None, "dom"),
        P(None, "dom"),
        P(None, "dom"),
    )
    return jax.shard_map(
        local, mesh=mesh, in_specs=placed, out_specs=P(None, None, "dom"), check_vma=False
    )
```
